768 devices in a mesh: row: 8 (over x, core), col: 96 (over y, z).
Axes of the slice: x: 4, y: 8, z: 12, core: 2. Of those that a mesh axis runs over, the one named last changes fastest.
Arguments:
- slab_blocks: bfloat16 [2048, 122880], P('row', 'col'), may hold values from -6 to 6
- slab_pattern: int32 [16, 960], P('row', 'col'), may hold values 0 or 1
- right_blocks: bfloat16 [122880, 3072], P('col', 'row'), may hold values from -0.0546875 to 0.0546875
- right_pattern: int32 [960, 24], P('col', 'row'), may hold values 0 or 1
- atom_sizes: int32 [960], P('col'), may hold values from 64 to 128
Outputs:
- product: float32 [2048, 3072], P('row', 'col')
The draws below stay inside these ranges and needn't reach their ends.
All inputs are finite; a program needn't handle non-finite values. No bound on the sum of `slab_pattern` or of `right_pattern` on one device may be relied on, other than what follows from the above.
Results may differ from the reference program's by a relative error of at most 0.0003.
Values may be sent and summed in bfloat16 or wider, within the bound.
No kernel may reach another device: no remote copies, remote signals or barrier semaphores. Data moves between devices by JAX's collectives and lax.ppermute only.
A program may use at most 32 MiB of HBM per device.

```python
import jax
import jax.numpy as jnp

BS = 128
RB = 16
KB = 960
NB = 24
R = 2048
K = 122880
N = 3072


def touch_ends(result, own_key, smallest, high):
    dims = result.shape
    index_at = [jax.random.randint(jax.random.fold_in(own_key, axis), (), 0, dims[axis]) for axis in range(len(dims))]
    result = result.at[tuple(index_at)].set(smallest)
    longest = dims.index(max(dims))
    index_at[longest] = (index_at[longest] + 1) % dims[longest]
    return result.at[tuple(index_at)].set(high)


def spiked(entries, key, source, target, shards_of, factor):
    owner, partner = [(jnp.arange(entries.shape[dim]) // (entries.shape[dim] // shards_of)).reshape([-1 if axis == dim else 1 for axis in range(entries.ndim)]) for dim in (source, target)]
    chosen = jax.random.permutation(key, shards_of)[partner]
    strong = (owner == chosen) | (owner == (partner + shards_of // 2) % shards_of)
    return jnp.where(strong, factor * entries, entries)


def shard_levels(own_key, extent, cuts, smallest, high):
    def one(position, blocks):
        draws = jax.random.uniform(jax.random.fold_in(jax.random.fold_in(own_key, 6), position), (blocks,), jnp.float32, smallest / len(cuts), high / len(cuts))
        return jnp.repeat(jnp.exp(draws), extent[position] // blocks).reshape((-1,) + (1,) * (len(extent) - position - 1))

    loudness = one(*cuts[0])
    for cut in cuts[1:]:
        loudness = loudness * one(*cut)
    return loudness


def gaussian(stream_key, extent, spread, limit, pieces=(), held_as=jnp.bfloat16):
    level = shard_levels(stream_key, extent, pieces, -0.22, 0.18) if pieces else 1.0
    entries = jax.random.normal(stream_key, extent, jnp.float32) * spread * level
    return jnp.minimum(jnp.maximum(entries, -limit), limit).astype(held_as)


def noise_with(own_key, dims, spread, bound, cuts, heavy, kind=jnp.bfloat16):
    array = spread * jax.random.normal(own_key, dims, jnp.float32)
    if cuts:
        array = array * shard_levels(own_key, dims, cuts, -0.22, 0.18)
    return jnp.clip(spiked(array, jax.random.fold_in(own_key, 3), *heavy), -bound, bound).astype(kind)


def setup_inputs(seed: int = 0) -> dict:
    keys = jax.random.split(jax.random.key(seed), 6)
    return {
        "slab_blocks": gaussian(keys[0], (R, K), 1.0, 6.0, ((0, 8), (1, 96))),
        "slab_pattern": touch_ends((jax.random.randint(keys[1], (RB, KB), 0, 3) < 2).astype(jnp.int32), jax.random.fold_in(keys[1], 1), 0, 1),
        "right_blocks": noise_with(keys[2], (K, N), K ** -0.5, 0.0546875, ((0, 96), (1, 8)), (0, 1, 96, 4.75)),
        "right_pattern": touch_ends((jax.random.randint(keys[3], (KB, NB), 0, 3) < 2).astype(jnp.int32), jax.random.fold_in(keys[3], 1), 0, 1),
        "atom_sizes": touch_ends(jax.random.randint(keys[4], (KB,), BS // 2, BS + 1), jax.random.fold_in(keys[4], 1), BS // 2, BS).astype(jnp.int32),
    }


def orbital_mask(sizes):
    inner = jnp.arange(BS, dtype=jnp.int32)
    return (inner[None, :] < sizes[:, None]).reshape(-1).astype(jnp.bfloat16)


def reference(slab_blocks, slab_pattern, right_blocks, right_pattern, atom_sizes):
    orbitals = orbital_mask(atom_sizes)
    left_mask = jnp.repeat(jnp.repeat(slab_pattern.astype(jnp.bfloat16), BS, axis=0), BS, axis=1)
    right_mask = jnp.repeat(jnp.repeat(right_pattern.astype(jnp.bfloat16), BS, axis=0), BS, axis=1)
    left = slab_blocks * left_mask * orbitals[None, :]
    right = right_blocks * right_mask * orbitals[:, None]
    return jnp.dot(left, right, preferred_element_type=jnp.float32)
```

```python
import jax
import jax.numpy as jnp
from jax import lax
from jax.sharding import Mesh, PartitionSpec as P

ZN = 12


def orbital_mask(sizes, width):
    inner = jnp.arange(width, dtype=jnp.int32)
    return (inner[None, :] < sizes[:, None]).reshape(-1).astype(jnp.bfloat16)


def shards(slab_blocks, slab_pattern, right_blocks, right_pattern, atom_sizes):
    width = slab_blocks.shape[1] // atom_sizes.shape[0]
    orbitals = orbital_mask(atom_sizes, width)
    left_mask = jnp.repeat(jnp.repeat(slab_pattern.astype(jnp.bfloat16), width, axis=0), width, axis=1)
    right_mask = jnp.repeat(jnp.repeat(right_pattern.astype(jnp.bfloat16), width, axis=0), width, axis=1)
    left = slab_blocks * left_mask * orbitals[None, :]
    right = right_blocks * right_mask * orbitals[:, None]
    partial = jnp.dot(left, lax.all_gather(right, "row", axis=1, tiled=True), preferred_element_type=jnp.float32)
    ny, nz = lax.axis_size("y"), lax.axis_size("z")
    rows, cols = partial.shape
    p = partial.reshape(rows, ny, nz, cols // (ny * nz))
    p = lax.psum_scatter(p, FIRST, scatter_dimension=AXES[FIRST], tiled=True)
    p = lax.psum_scatter(p, SECOND, scatter_dimension=AXES[SECOND], tiled=True)
    return p.reshape(rows, -1)


AXES = {"y": 1, "z": 2}
FIRST, SECOND = "y", "z"


def solution(mesh):
    nr, nc = mesh.devices.shape
    view = Mesh(mesh.devices.reshape(nr, nc // ZN, ZN), ("row", "y", "z"))
    col = ("y", "z")
    in_specs = (P("row", col), P("row", col), P(col, "row"), P(col, "row"), P(col))
    out_specs = P("row", col)
    return jax.shard_map(shards, mesh=view, in_specs=in_specs, out_specs=out_specs, check_vma=False)
```

```python
import jax
import jax.numpy as jnp
from jax import lax
from jax.sharding import Mesh, PartitionSpec as P

XN, ZN = 4, 12
GATHER = "flat"
STAGE2 = "a2a"


def orbital_mask(sizes, width):
    inner = jnp.arange(width, dtype=jnp.int32)
    return (inner[None, :] < sizes[:, None]).reshape(-1).astype(jnp.bfloat16)


def gather_right(right):
    if GATHER == "flat":
        return lax.all_gather(right, ("x", "core"), axis=1, tiled=True), False
    g = lax.all_gather(right, "x", axis=1, tiled=True)
    return lax.all_gather(g, "core", axis=1, tiled=True), True


def shards(slab_blocks, slab_pattern, right_blocks, right_pattern, atom_sizes):
    width = slab_blocks.shape[1] // atom_sizes.shape[0]
    orbitals = orbital_mask(atom_sizes, width)
    left_mask = jnp.repeat(jnp.repeat(slab_pattern.astype(jnp.bfloat16), width, axis=0), width, axis=1)
    right_mask = jnp.repeat(jnp.repeat(right_pattern.astype(jnp.bfloat16), width, axis=0), width, axis=1)
    left = slab_blocks * left_mask * orbitals[None, :]
    right = right_blocks * right_mask * orbitals[:, None]
    gathered, swapped = gather_right(right)
    partial = jnp.dot(left, gathered, preferred_element_type=jnp.float32)
    rows, cols = partial.shape
    nx, nk = lax.axis_size("x"), lax.axis_size("core")
    if swapped:
        partial = partial.reshape(rows, nk, nx, cols // (nk * nx)).transpose(0, 2, 1, 3)
    ny, nz = lax.axis_size("y"), lax.axis_size("z")
    p = partial.reshape(rows, ny, nz, cols // (ny * nz))
    p = lax.psum_scatter(p, "y", scatter_dimension=1, tiled=True)
    if STAGE2 == "rs":
        p = lax.psum_scatter(p, "z", scatter_dimension=2, tiled=True)
    elif STAGE2 == "a2a":
        p = lax.all_to_all(p, "z", 2, 2, tiled=True).sum(axis=2, keepdims=True)
    elif STAGE2 == "ar":
        p = lax.dynamic_slice_in_dim(lax.psum(p, "z"), lax.axis_index("z"), 1, axis=2)
    return p.reshape(rows, -1)


def solution(mesh):
    nr, nc = mesh.devices.shape
    view = Mesh(mesh.devices.reshape(XN, nr // XN, nc // ZN, ZN), ("x", "core", "y", "z"))
    row, col = ("x", "core"), ("y", "z")
    in_specs = (P(row, col), P(row, col), P(col, row), P(col, row), P(col))
    out_specs = P(row, col)
    return jax.shard_map(shards, mesh=view, in_specs=in_specs, out_specs=out_specs, check_vma=False)
```
